1024 devices in a mesh: dp: 64 (over y, z), sub: 16 (over x, core).
Axes of the slice: x: 8, y: 8, z: 8, core: 2. Of those that a mesh axis runs over, the one named last changes fastest.
Arguments:
- activations: bfloat16 [196608, 5632], P(('dp', 'sub')), may hold values from -6 to 6
- grad_out: bfloat16 [196608, 1408], P(('dp', 'sub'))
- q_prev: bfloat16 [1408, 32], replicated, may hold values from -0.15625 to 0.15625
Outputs:
- grad_approx: float32 [5632, 1408], P('sub')
- q_new: float32 [1408, 32], replicated
The draws below stay inside these ranges and needn't reach their ends.
All inputs are finite; a program needn't handle non-finite values.
Results may differ from the reference program's by a relative error of at most 0.0036.
Values may be sent and summed in bfloat16 or wider, within the bound.
No kernel may reach another device: no remote copies, remote signals or barrier semaphores. Data moves between devices by JAX's collectives and lax.ppermute only.
A program may use at most 32 MiB of HBM per device.

```python
import math
import jax
import jax.numpy as jnp
from jax import lax

C = 1408
FF = 5632
R = 32
TOK_DEV = 192
TOKENS = 196608
N_DP = 64
N_SUB = 16


def draw_grad_out(key, part):
    first = jax.random.fold_in(key, 0)
    place = jnp.arange(TOKENS, dtype=jnp.float32) / TOKENS
    rising = jnp.exp(place * math.log(10.0))[:, None]
    values = jnp.clip(jax.random.normal(first, (TOKENS, C), jnp.float32), -6.0, 6.0) * rising
    return values.astype(jnp.bfloat16)


def level_of(stream_key, shape, shards, low, top_value):
    def one(position, blocks):
        steps = jax.random.uniform(jax.random.fold_in(jax.random.fold_in(stream_key, 6), position), (blocks,), jnp.float32, low / len(shards), top_value / len(shards))
        return jnp.repeat(jnp.exp(steps), shape[position] // blocks).reshape((-1,) + (1,) * (len(shape) - position - 1))

    gain = one(*shards[0])
    for cut in shards[1:]:
        gain = gain * one(*cut)
    return gain


def centred(own_key, shape, deviation, most, shards=(), held_as=jnp.bfloat16):
    gain = level_of(own_key, shape, shards, -0.22, 0.18) if shards else 1.0
    values = jax.random.normal(own_key, shape, jnp.float32) * deviation * gain
    return jnp.minimum(jnp.maximum(values, -most), most).astype(held_as)


def setup_inputs(seed: int = 0) -> dict:
    keys = jax.random.split(jax.random.key(seed), 4)
    return {
        "activations": centred(keys[0], (TOKENS, FF), 1.0, 6.0, ((0, 1024),)),
        "grad_out": draw_grad_out(jax.random.fold_in(keys[3], 71), 0),
        "q_prev": centred(keys[2], (C, R), C ** -0.5, 0.15625),
    }


def reference(activations, grad_out, q_prev):
    count = N_DP * N_SUB
    act_blocks = activations.reshape(count, TOK_DEV, FF)
    out_blocks = grad_out.reshape(count, TOK_DEV, C)

    def left_step(total, pair):
        act_block, out_block = pair
        u_part = jnp.dot(out_block.astype(jnp.float32), q_prev.astype(jnp.float32), preferred_element_type=jnp.float32).astype(jnp.bfloat16)
        return (total + jnp.dot(act_block.T.astype(jnp.float32), u_part.astype(jnp.float32), preferred_element_type=jnp.float32), None)
    p_sum, _ = lax.scan(left_step, jnp.zeros((FF, R), jnp.float32), (act_blocks, out_blocks))
    gram = jnp.dot(p_sum.T, p_sum, precision=lax.Precision.HIGHEST)
    lower = lax.linalg.cholesky(gram)
    p_hat = lax.linalg.triangular_solve(lower, p_sum, left_side=False, lower=True, transpose_a=True)
    p_low = p_hat.astype(jnp.bfloat16)

    def right_step(total, pair):
        act_block, out_block = pair
        v_part = jnp.dot(act_block.astype(jnp.float32), p_low.astype(jnp.float32), preferred_element_type=jnp.float32).astype(jnp.bfloat16)
        return (total + jnp.dot(out_block.T.astype(jnp.float32), v_part.astype(jnp.float32), preferred_element_type=jnp.float32), None)
    q_sum, _ = lax.scan(right_step, jnp.zeros((C, R), jnp.float32), (act_blocks, out_blocks))
    q_new = q_sum / count
    grad_approx = jnp.dot(p_hat, q_new.T, precision=lax.Precision.HIGHEST)
    return (grad_approx, q_new)
```

```python
import jax
import jax.numpy as jnp
from jax import lax
from jax.sharding import PartitionSpec as P

AXES = ("dp", "sub")


def exchange_order(n_dp, n_sub):
    core_bits = [0]
    sub_bits = list(range(1, (n_sub // 2).bit_length()))
    dp_len = n_dp.bit_length() - 1
    z_bits = [n_sub.bit_length() - 1 + k for k in range(dp_len // 2)]
    y_bits = [z_bits[-1] + 1 + k for k in range(dp_len - len(z_bits))]
    order = list(core_bits)
    for level in range(max(len(sub_bits), len(z_bits), len(y_bits))):
        for bits in (sub_bits, z_bits, y_bits):
            if level < len(bits):
                order.append(bits[level])
    return order


def xor_pairs(n, bit):
    return [(i, i ^ (1 << bit)) for i in range(n)]


def butterfly_sum(x, order, n, max_halvings):
    idx = lax.axis_index(AXES)
    halved = []
    for bit in order:
        rows = x.shape[0]
        if len(halved) < max_halvings and rows % 16 == 0:
            half = rows // 2
            mine = (idx >> bit) & 1
            lo, hi = x[:half], x[half:]
            send = jnp.where(mine == 1, lo, hi)
            keep = jnp.where(mine == 1, hi, lo)
            x = keep + lax.ppermute(send, AXES, xor_pairs(n, bit))
            halved.append(bit)
        else:
            x = x + lax.ppermute(x, AXES, xor_pairs(n, bit))
    for bit in reversed(halved):
        mine = (idx >> bit) & 1
        other = lax.ppermute(x, AXES, xor_pairs(n, bit))
        x = jnp.where(mine == 1, jnp.concatenate([other, x]), jnp.concatenate([x, other]))
    return x


def orthonormal(rows_part, gram):
    lower = lax.linalg.cholesky(gram)
    return lax.linalg.triangular_solve(
        lower, rows_part, left_side=False, lower=True, transpose_a=True
    )


def make_per_device(n_dp, n_sub):
    n = n_dp * n_sub
    order = exchange_order(n_dp, n_sub)

    def per_device(activations, grad_out, q_prev):
        u_low = jnp.dot(grad_out, q_prev, preferred_element_type=jnp.float32).astype(jnp.bfloat16)
        p_local = jnp.einsum("tf,tr->fr", activations, u_low, preferred_element_type=jnp.float32)
        hidden = activations.shape[1]
        block_rows = hidden // n_sub
        p_sum = butterfly_sum(p_local, order, n, 5)
        gram = jnp.dot(p_sum.T, p_sum, precision=lax.Precision.HIGHEST)
        p_hat = orthonormal(p_sum, gram)
        p_low = p_hat.astype(jnp.bfloat16)
        my_hat = lax.dynamic_slice_in_dim(p_hat, lax.axis_index("sub") * block_rows, block_rows, 0)
        v_low = jnp.dot(activations, p_low, preferred_element_type=jnp.float32).astype(jnp.bfloat16)
        q_local = jnp.einsum("tc,tr->cr", grad_out, v_low, preferred_element_type=jnp.float32)
        q_sum = butterfly_sum(q_local, order, n, 3)
        q_new = q_sum / n
        grad_approx = jnp.dot(my_hat, q_new.T, precision=lax.Precision.HIGHEST)
        return (grad_approx, q_new)

    return per_device


def solution(mesh):
    in_specs = (P(AXES, None), P(AXES, None), P())
    out_specs = (P("sub", None), P())
    per_device = make_per_device(mesh.shape["dp"], mesh.shape["sub"])
    return jax.shard_map(
        per_device, mesh=mesh, in_specs=in_specs, out_specs=out_specs, check_vma=False
    )
```

```python
import jax
import jax.numpy as jnp
from jax import lax
from jax.sharding import PartitionSpec as P

AXES = ("dp", "sub")


def exchange_order(n_dp, n_sub):
    core_bits = [0]
    sub_bits = list(range(1, (n_sub // 2).bit_length()))
    dp_len = n_dp.bit_length() - 1
    z_bits = [n_sub.bit_length() - 1 + k for k in range(dp_len // 2)]
    y_bits = [z_bits[-1] + 1 + k for k in range(dp_len - len(z_bits))]
    order = list(core_bits)
    for level in range(max(len(sub_bits), len(z_bits), len(y_bits))):
        for bits in (sub_bits, z_bits, y_bits):
            if level < len(bits):
                order.append(bits[level])
    return order


def xor_pairs(n, bit):
    return [(i, i ^ (1 << bit)) for i in range(n)]


def butterfly_sum(x, order, n, max_halvings):
    idx = lax.axis_index(AXES)
    halved = []
    for bit in order:
        rows = x.shape[0]
        if len(halved) < max_halvings and rows % 16 == 0:
            half = rows // 2
            mine = (idx >> bit) & 1
            lo, hi = x[:half], x[half:]
            send = jnp.where(mine == 1, lo, hi)
            keep = jnp.where(mine == 1, hi, lo)
            x = keep + lax.ppermute(send, AXES, xor_pairs(n, bit))
            halved.append(bit)
        else:
            x = x + lax.ppermute(x, AXES, xor_pairs(n, bit))
    for bit in reversed(halved):
        mine = (idx >> bit) & 1
        other = lax.ppermute(x, AXES, xor_pairs(n, bit))
        x = jnp.where(mine == 1, jnp.concatenate([other, x]), jnp.concatenate([x, other]))
    return x


def orthonormal(rows_part, gram):
    lower = lax.linalg.cholesky(gram)
    return lax.linalg.triangular_solve(
        lower, rows_part, left_side=False, lower=True, transpose_a=True
    )


def make_per_device(n_dp, n_sub):
    n = n_dp * n_sub
    order = exchange_order(n_dp, n_sub)

    def per_device(activations, grad_out, q_prev):
        u_low = jnp.dot(grad_out, q_prev, preferred_element_type=jnp.float32).astype(jnp.bfloat16)
        p_local = jnp.einsum("tf,tr->fr", activations, u_low, preferred_element_type=jnp.float32)
        hidden = activations.shape[1]
        block_rows = hidden // n_sub
        p_sum = butterfly_sum(p_local, order, n, 5)
        gram = jnp.dot(p_sum.T, p_sum, precision=lax.Precision.HIGH)
        p_hat = orthonormal(p_sum, gram)
        p_low = p_hat.astype(jnp.bfloat16)
        my_hat = lax.dynamic_slice_in_dim(p_hat, lax.axis_index("sub") * block_rows, block_rows, 0)
        v_low = jnp.dot(activations, p_low, preferred_element_type=jnp.float32).astype(jnp.bfloat16)
        q_local = jnp.einsum("tc,tr->cr", grad_out, v_low, preferred_element_type=jnp.float32)
        q_sum = butterfly_sum(q_local, order, n, 3)
        q_new = q_sum / n
        grad_approx = jnp.dot(my_hat, q_new.T, precision=lax.Precision.HIGH)
        return (grad_approx, q_new)

    return per_device


def solution(mesh):
    in_specs = (P(AXES, None), P(AXES, None), P())
    out_specs = (P("sub", None), P())
    per_device = make_per_device(mesh.shape["dp"], mesh.shape["sub"])
    return jax.shard_map(
        per_device, mesh=mesh, in_specs=in_specs, out_specs=out_specs, check_vma=False
    )
```

```python
import jax
import jax.numpy as jnp
from jax import lax
from jax.sharding import PartitionSpec as P

AXES = ("dp", "sub")


def exchange_order(n_dp, n_sub):
    core_bits = [0]
    sub_bits = list(range(1, (n_sub // 2).bit_length()))
    dp_len = n_dp.bit_length() - 1
    z_bits = [n_sub.bit_length() - 1 + k for k in range(dp_len // 2)]
    y_bits = [z_bits[-1] + 1 + k for k in range(dp_len - len(z_bits))]
    order = list(core_bits)
    for level in range(max(len(sub_bits), len(z_bits), len(y_bits))):
        for bits in (sub_bits, z_bits, y_bits):
            if level < len(bits):
                order.append(bits[level])
    return order


def xor_pairs(n, bit):
    return [(i, i ^ (1 << bit)) for i in range(n)]


def group_pairs(n, bits, t):
    mask = sum(1 << b for k, b in enumerate(bits) if (t >> k) & 1)
    return [(i, i ^ mask) for i in range(n)]


def butterfly_sum(x, order, n, max_halvings, first_group=2):
    idx = lax.axis_index(AXES)
    group, rest = order[:first_group], order[first_group:]
    parts = 1 << len(group)
    c = sum(((idx >> b) & 1) << k for k, b in enumerate(group))
    piece = x.shape[0] // parts
    acc = lax.dynamic_slice_in_dim(x, c * piece, piece, 0)
    for t in range(1, parts):
        send = lax.dynamic_slice_in_dim(x, (c ^ t) * piece, piece, 0)
        acc = acc + lax.ppermute(send, AXES, group_pairs(n, group, t))
    x = acc
    halved = []
    for bit in rest:
        rows = x.shape[0]
        if len(halved) + len(group) < max_halvings and rows % 16 == 0:
            half = rows // 2
            mine = (idx >> bit) & 1
            lo, hi = x[:half], x[half:]
            send = jnp.where(mine == 1, lo, hi)
            keep = jnp.where(mine == 1, hi, lo)
            x = keep + lax.ppermute(send, AXES, xor_pairs(n, bit))
            halved.append(bit)
        else:
            x = x + lax.ppermute(x, AXES, xor_pairs(n, bit))
    for bit in reversed(halved):
        mine = (idx >> bit) & 1
        other = lax.ppermute(x, AXES, xor_pairs(n, bit))
        x = jnp.where(mine == 1, jnp.concatenate([other, x]), jnp.concatenate([x, other]))
    out = jnp.zeros((parts * x.shape[0],) + x.shape[1:], x.dtype)
    out = lax.dynamic_update_slice_in_dim(out, x, c * x.shape[0], 0)
    for t in range(1, parts):
        got = lax.ppermute(x, AXES, group_pairs(n, group, t))
        out = lax.dynamic_update_slice_in_dim(out, got, (c ^ t) * x.shape[0], 0)
    return out


def orthonormal(rows_part, gram):
    lower = lax.linalg.cholesky(gram)
    return lax.linalg.triangular_solve(
        lower, rows_part, left_side=False, lower=True, transpose_a=True
    )


def make_per_device(n_dp, n_sub):
    n = n_dp * n_sub
    order = exchange_order(n_dp, n_sub)

    def per_device(activations, grad_out, q_prev):
        u_low = jnp.dot(grad_out, q_prev, preferred_element_type=jnp.float32).astype(jnp.bfloat16)
        p_local = jnp.einsum("tf,tr->fr", activations, u_low, preferred_element_type=jnp.float32)
        hidden = activations.shape[1]
        block_rows = hidden // n_sub
        p_sum = butterfly_sum(p_local, order, n, 5)
        gram = jnp.dot(p_sum.T, p_sum, precision=lax.Precision.HIGH)
        p_hat = orthonormal(p_sum, gram)
        p_low = p_hat.astype(jnp.bfloat16)
        my_hat = lax.dynamic_slice_in_dim(p_hat, lax.axis_index("sub") * block_rows, block_rows, 0)
        v_low = jnp.dot(activations, p_low, preferred_element_type=jnp.float32).astype(jnp.bfloat16)
        q_local = jnp.einsum("tc,tr->cr", grad_out, v_low, preferred_element_type=jnp.float32)
        q_sum = butterfly_sum(q_local, order, n, 3)
        q_new = q_sum / n
        grad_approx = jnp.dot(my_hat, q_new.T, precision=lax.Precision.HIGH)
        return (grad_approx, q_new)

    return per_device


def solution(mesh):
    in_specs = (P(AXES, None), P(AXES, None), P())
    out_specs = (P("sub", None), P())
    per_device = make_per_device(mesh.shape["dp"], mesh.shape["sub"])
    return jax.shard_map(
        per_device, mesh=mesh, in_specs=in_specs, out_specs=out_specs, check_vma=False
    )
```

```python
import jax
import jax.numpy as jnp
from jax import lax
from jax.sharding import PartitionSpec as P

AXES = ("dp", "sub")


def exchange_order(n_dp, n_sub):
    core_bits = [0]
    sub_bits = list(range(1, (n_sub // 2).bit_length()))
    dp_len = n_dp.bit_length() - 1
    z_bits = [n_sub.bit_length() - 1 + k for k in range(dp_len // 2)]
    y_bits = [z_bits[-1] + 1 + k for k in range(dp_len - len(z_bits))]
    order = list(core_bits)
    for level in range(max(len(sub_bits), len(z_bits), len(y_bits))):
        for bits in (sub_bits, z_bits, y_bits):
            if level < len(bits):
                order.append(bits[level])
    return order


def xor_pairs(n, bit):
    return [(i, i ^ (1 << bit)) for i in range(n)]


def butterfly_sum(x, order, n, max_halvings):
    idx = lax.axis_index(AXES)
    halved = []
    for bit in order:
        rows = x.shape[0]
        if len(halved) < max_halvings and rows % 16 == 0:
            half = rows // 2
            mine = (idx >> bit) & 1
            send = lax.dynamic_slice_in_dim(x, (1 - mine) * half, half, 0)
            keep = lax.dynamic_slice_in_dim(x, mine * half, half, 0)
            x = keep + lax.ppermute(send, AXES, xor_pairs(n, bit))
            halved.append(bit)
        else:
            x = x + lax.ppermute(x, AXES, xor_pairs(n, bit))
    for bit in reversed(halved):
        mine = (idx >> bit) & 1
        other = lax.ppermute(x, AXES, xor_pairs(n, bit))
        x = lax.dynamic_update_slice_in_dim(jnp.concatenate([other, other]), x, mine * x.shape[0], 0)
    return x


def orthonormal(rows_part, gram):
    lower = lax.linalg.cholesky(gram)
    return lax.linalg.triangular_solve(
        lower, rows_part, left_side=False, lower=True, transpose_a=True
    )


def make_per_device(n_dp, n_sub):
    n = n_dp * n_sub
    order = exchange_order(n_dp, n_sub)

    def per_device(activations, grad_out, q_prev):
        u_low = jnp.dot(grad_out, q_prev, preferred_element_type=jnp.float32).astype(jnp.bfloat16)
        p_local = jnp.einsum("tf,tr->fr", activations, u_low, preferred_element_type=jnp.float32)
        hidden = activations.shape[1]
        block_rows = hidden // n_sub
        p_sum = butterfly_sum(p_local, order, n, 5)
        gram = jnp.dot(p_sum.T, p_sum, precision=lax.Precision.HIGH)
        p_hat = orthonormal(p_sum, gram)
        p_low = p_hat.astype(jnp.bfloat16)
        my_hat = lax.dynamic_slice_in_dim(p_hat, lax.axis_index("sub") * block_rows, block_rows, 0)
        v_low = jnp.dot(activations, p_low, preferred_element_type=jnp.float32).astype(jnp.bfloat16)
        q_local = jnp.einsum("tc,tr->cr", grad_out, v_low, preferred_element_type=jnp.float32)
        q_sum = butterfly_sum(q_local, order, n, 3)
        q_new = q_sum / n
        grad_approx = jnp.dot(my_hat, q_new.T, precision=lax.Precision.HIGH)
        return (grad_approx, q_new)

    return per_device


def solution(mesh):
    in_specs = (P(AXES, None), P(AXES, None), P())
    out_specs = (P("sub", None), P())
    per_device = make_per_device(mesh.shape["dp"], mesh.shape["sub"])
    return jax.shard_map(
        per_device, mesh=mesh, in_specs=in_specs, out_specs=out_specs, check_vma=False
    )
```

```python
import jax
import jax.numpy as jnp
from jax import lax
from jax.sharding import PartitionSpec as P

AXES = ("dp", "sub")


def exchange_order(n_dp, n_sub):
    core_bits = [0]
    sub_bits = list(range(1, (n_sub // 2).bit_length()))
    dp_len = n_dp.bit_length() - 1
    z_bits = [n_sub.bit_length() - 1 + k for k in range(dp_len // 2)]
    y_bits = [z_bits[-1] + 1 + k for k in range(dp_len - len(z_bits))]
    order = list(core_bits)
    for level in range(max(len(sub_bits), len(z_bits), len(y_bits))):
        for bits in (sub_bits, z_bits, y_bits):
            if level < len(bits):
                order.append(bits[level])
    return order


def xor_pairs(n, bit):
    return [(i, i ^ (1 << bit)) for i in range(n)]


def butterfly_sum(x, order, n, max_halvings):
    idx = lax.axis_index(AXES)
    halved = []
    for bit in order:
        rows = x.shape[0]
        if len(halved) < max_halvings and rows % 16 == 0:
            half = rows // 2
            mine = (idx >> bit) & 1
            lo, hi = x[:half], x[half:]
            send = jnp.where(mine == 1, lo, hi)
            keep = jnp.where(mine == 1, hi, lo)
            x = keep + lax.ppermute(send, AXES, xor_pairs(n, bit))
            halved.append(bit)
        else:
            x = x + lax.ppermute(x, AXES, xor_pairs(n, bit))
    for bit in reversed(halved):
        mine = (idx >> bit) & 1
        other = lax.ppermute(x, AXES, xor_pairs(n, bit))
        x = jnp.where(mine == 1, jnp.concatenate([other, x]), jnp.concatenate([x, other]))
    return x


def orthonormal(rows_part, gram):
    lower = lax.linalg.cholesky(gram)
    return lax.linalg.triangular_solve(
        lower, rows_part, left_side=False, lower=True, transpose_a=True
    )


def make_per_device(n_dp, n_sub):
    n = n_dp * n_sub
    order = exchange_order(n_dp, n_sub)

    def per_device(activations, grad_out, q_prev):
        u_low = jnp.dot(grad_out, q_prev, preferred_element_type=jnp.float32).astype(jnp.bfloat16)
        p_local = jnp.einsum("tf,tr->fr", activations, u_low, preferred_element_type=jnp.float32)
        hidden = activations.shape[1]
        block_rows = hidden // n_sub
        p_sum = butterfly_sum(p_local, order, n, 5)
        gram = jnp.dot(p_sum.T, p_sum, precision=lax.Precision.HIGH)
        p_hat = orthonormal(p_sum, gram)
        p_low = p_hat.astype(jnp.bfloat16)
        my_hat = lax.dynamic_slice_in_dim(p_hat, lax.axis_index("sub") * block_rows, block_rows, 0)
        v_low = jnp.dot(activations, p_low, preferred_element_type=jnp.float32).astype(jnp.bfloat16)
        q_local = jnp.einsum("tc,tr->cr", grad_out, v_low, preferred_element_type=jnp.float32)
        q_sum = butterfly_sum(q_local, order, n, 4)
        q_new = q_sum / n
        grad_approx = jnp.dot(my_hat, q_new.T, precision=lax.Precision.HIGH)
        return (grad_approx, q_new)

    return per_device


def solution(mesh):
    in_specs = (P(AXES, None), P(AXES, None), P())
    out_specs = (P("sub", None), P())
    per_device = make_per_device(mesh.shape["dp"], mesh.shape["sub"])
    return jax.shard_map(
        per_device, mesh=mesh, in_specs=in_specs, out_specs=out_specs, check_vma=False
    )
```

```python
import jax
import jax.numpy as jnp
from jax import lax
from jax.sharding import PartitionSpec as P

AXES = ("dp", "sub")


def exchange_order(n_dp, n_sub):
    core_bits = [0]
    sub_bits = list(range(1, (n_sub // 2).bit_length()))
    dp_len = n_dp.bit_length() - 1
    z_bits = [n_sub.bit_length() - 1 + k for k in range(dp_len // 2)]
    y_bits = [z_bits[-1] + 1 + k for k in range(dp_len - len(z_bits))]
    order = list(core_bits)
    for level in range(max(len(sub_bits), len(z_bits), len(y_bits))):
        for bits in (sub_bits, z_bits, y_bits):
            if level < len(bits):
                order.append(bits[level])
    return order


def xor_pairs(n, bit):
    return [(i, i ^ (1 << bit)) for i in range(n)]


def butterfly_sum(x, order, n, max_halvings):
    idx = lax.axis_index(AXES)
    halved = []
    for bit in order:
        rows = x.shape[0]
        if len(halved) < max_halvings and rows % 16 == 0:
            half = rows // 2
            mine = (idx >> bit) & 1
            lo, hi = x[:half], x[half:]
            send = jnp.where(mine == 1, lo, hi)
            keep = jnp.where(mine == 1, hi, lo)
            x = keep + lax.ppermute(send, AXES, xor_pairs(n, bit))
            halved.append(bit)
        else:
            x = x + lax.ppermute(x, AXES, xor_pairs(n, bit))
    for bit in reversed(halved):
        mine = (idx >> bit) & 1
        other = lax.ppermute(x, AXES, xor_pairs(n, bit))
        x = jnp.where(mine == 1, jnp.concatenate([other, x]), jnp.concatenate([x, other]))
    return x


def orthonormal(rows_part, gram):
    lower = lax.linalg.cholesky(gram)
    return lax.linalg.triangular_solve(
        lower, rows_part, left_side=False, lower=True, transpose_a=True
    )


def make_per_device(n_dp, n_sub):
    n = n_dp * n_sub
    order = exchange_order(n_dp, n_sub)

    def per_device(activations, grad_out, q_prev):
        u_low = jnp.dot(grad_out, q_prev, preferred_element_type=jnp.float32).astype(jnp.bfloat16)
        p_local = jnp.einsum("tf,tr->fr", activations, u_low, preferred_element_type=jnp.float32)
        hidden = activations.shape[1]
        block_rows = hidden // n_sub
        p_sum = butterfly_sum(p_local, order, n, 4)
        gram = jnp.dot(p_sum.T, p_sum, precision=lax.Precision.HIGH)
        p_hat = orthonormal(p_sum, gram)
        p_low = p_hat.astype(jnp.bfloat16)
        my_hat = lax.dynamic_slice_in_dim(p_hat, lax.axis_index("sub") * block_rows, block_rows, 0)
        v_low = jnp.dot(activations, p_low, preferred_element_type=jnp.float32).astype(jnp.bfloat16)
        q_local = jnp.einsum("tc,tr->cr", grad_out, v_low, preferred_element_type=jnp.float32)
        q_sum = butterfly_sum(q_local, order, n, 3)
        q_new = q_sum / n
        grad_approx = jnp.dot(my_hat, q_new.T, precision=lax.Precision.HIGH)
        return (grad_approx, q_new)

    return per_device


def solution(mesh):
    in_specs = (P(AXES, None), P(AXES, None), P())
    out_specs = (P("sub", None), P())
    per_device = make_per_device(mesh.shape["dp"], mesh.shape["sub"])
    return jax.shard_map(
        per_device, mesh=mesh, in_specs=in_specs, out_specs=out_specs, check_vma=False
    )
```

```python
import jax
import jax.numpy as jnp
from jax import lax
from jax.sharding import PartitionSpec as P

AXES = ("dp", "sub")


def exchange_order(n_dp, n_sub):
    core_bits = [0]
    sub_bits = list(range(1, (n_sub // 2).bit_length()))
    dp_len = n_dp.bit_length() - 1
    z_bits = [n_sub.bit_length() - 1 + k for k in range(dp_len // 2)]
    y_bits = [z_bits[-1] + 1 + k for k in range(dp_len - len(z_bits))]
    order = list(core_bits)
    for level in range(max(len(sub_bits), len(z_bits), len(y_bits))):
        for bits in (sub_bits, z_bits, y_bits):
            if level < len(bits):
                order.append(bits[level])
    return order


def xor_pairs(n, bit):
    return [(i, i ^ (1 << bit)) for i in range(n)]


def butterfly_sum(x, order, n, max_halvings):
    idx = lax.axis_index(AXES)
    halved = []
    for bit in order:
        rows = x.shape[0]
        if len(halved) < max_halvings and rows % 16 == 0:
            half = rows // 2
            mine = (idx >> bit) & 1
            lo, hi = x[:half], x[half:]
            send = jnp.where(mine == 1, lo, hi)
            keep = jnp.where(mine == 1, hi, lo)
            x = keep + lax.ppermute(send, AXES, xor_pairs(n, bit))
            halved.append(bit)
        else:
            x = x + lax.ppermute(x, AXES, xor_pairs(n, bit))
    for bit in reversed(halved):
        mine = (idx >> bit) & 1
        other = lax.ppermute(x, AXES, xor_pairs(n, bit))
        x = jnp.where(mine == 1, jnp.concatenate([other, x]), jnp.concatenate([x, other]))
    return x


def orthonormal(rows_part, gram):
    lower = lax.linalg.cholesky(gram)
    return lax.linalg.triangular_solve(
        lower, rows_part, left_side=False, lower=True, transpose_a=True
    )


def make_per_device(n_dp, n_sub):
    n = n_dp * n_sub
    order = exchange_order(n_dp, n_sub)

    def per_device(activations, grad_out, q_prev):
        u_low = jnp.dot(grad_out, q_prev, preferred_element_type=jnp.float32).astype(jnp.bfloat16)
        p_local = jnp.einsum("tf,tr->fr", activations, u_low, preferred_element_type=jnp.float32)
        hidden = activations.shape[1]
        block_rows = hidden // n_sub
        p_sum = butterfly_sum(p_local, order, n, 4)
        gram = jnp.dot(p_sum.T, p_sum, precision=lax.Precision.HIGH)
        p_hat = orthonormal(p_sum, gram)
        p_low = p_hat.astype(jnp.bfloat16)
        my_hat = lax.dynamic_slice_in_dim(p_hat, lax.axis_index("sub") * block_rows, block_rows, 0)
        v_low = jnp.dot(activations, p_low, preferred_element_type=jnp.float32).astype(jnp.bfloat16)
        q_local = jnp.einsum("tc,tr->cr", grad_out, v_low, preferred_element_type=jnp.float32)
        q_sum = butterfly_sum(q_local, order, n, 2)
        q_new = q_sum / n
        grad_approx = jnp.dot(my_hat, q_new.T, precision=lax.Precision.HIGH)
        return (grad_approx, q_new)

    return per_device


def solution(mesh):
    in_specs = (P(AXES, None), P(AXES, None), P())
    out_specs = (P("sub", None), P())
    per_device = make_per_device(mesh.shape["dp"], mesh.shape["sub"])
    return jax.shard_map(
        per_device, mesh=mesh, in_specs=in_specs, out_specs=out_specs, check_vma=False
    )
```
